256 devices in a mesh: dp: 8 (over y, core), tm: 32 (over z, x).
Axes of the slice: x: 4, y: 4, z: 8, core: 2. Of those that a mesh axis runs over, the one named last changes fastest.
Arguments:
- window: bfloat16 [1024, 512, 512], P('tm', 'dp'), may hold values from -6 to 6
- link_ids: int32 [1024, 512], P('tm', 'dp'), may hold values from 0 to 63
- knot_ids: int32 [1024, 512], P('tm', 'dp'), may hold values from 0 to 511, as said below
- lag_steps: int32 [4], replicated, may hold values from 1 to 7, as said below
- topology: int32 [64, 64], replicated, may hold values 0 or 1
- smooth: float32 [256], replicated, may hold values from 200 to 6000
Outputs:
- scaled_coefs: float32 [512, 256], P(('dp', 'tm'))
The draws below stay inside these ranges and needn't reach their ends.
Inputs may be any that keep to these rules, and one draw needn't show every extreme that they name: `knot_ids`: the sample in row a and column b of the sample grid belongs to a knot k with k // 64 = (b % 64) // 8 and (k % 64) // 2 = a // 32: each device's columns come in 8 blocks of 8, block i holding samples of knots of the i-th index of dp. `lag_steps`: the lags are distinct; 1 and 7 are among them.
All inputs are finite; a program needn't handle non-finite values.
Results may differ from the reference program's by a relative error of at most 0.0019.
Values may be sent and summed in bfloat16 or wider, within the bound.
No kernel may reach another device: no remote copies, remote signals or barrier semaphores. Data moves between devices by JAX's collectives and lax.ppermute only.
A program may use at most 128 MiB of HBM per device.

```python
import math
import jax
import jax.numpy as jnp
from jax import lax

GROUPS = 64
NLAG = 4
WIN = 8
KPD = 2
RT = 32
RD = 64
COEFS = 256
DEST = 8
SPAN = 64
ROWS_TM = 1024
ROWS_DP = 512
KNOTS = 512
N_DP = 8
N_TM = 32


def draw_knot_ids(key, part):
    rows = jnp.arange(ROWS_TM)[:, None]
    cols = jnp.arange(ROWS_DP)[None, :]
    owner = cols % RD // DEST
    column = rows // RT
    within = jax.random.randint(key, (ROWS_TM, ROWS_DP), 0, KPD)
    return (owner * SPAN + column * KPD + within).astype(jnp.int32)


def draw_lag_steps(key, part):
    middle = jax.random.permutation(jax.random.fold_in(key, 11), WIN - 3) + 2
    chosen = jnp.concatenate([jnp.array([1, WIN - 1]), middle[:NLAG - 2]])
    order = jax.random.permutation(jax.random.fold_in(key, 23), NLAG)
    return chosen[order].astype(jnp.int32)


def set_ends(result, rng, smallest, largest):
    place = [jax.random.randint(jax.random.fold_in(rng, axis), (), 0, length) for axis, length in enumerate(result.shape)]
    widest = result.shape.index(max(result.shape))
    beside = place[:widest] + [(place[widest] + 1) % result.shape[widest]] + place[widest + 1:]
    return result.at[tuple(place)].set(smallest).at[tuple(beside)].set(largest)


def shard_levels(rng, extent, split, least, largest):
    gain = 1.0
    for dim, shards_of in split:
        draws = jax.random.uniform(jax.random.fold_in(jax.random.fold_in(rng, 6), dim), (shards_of,), jnp.float32, least / len(split), largest / len(split))
        gain = gain * jnp.repeat(jnp.exp(draws), extent[dim] // shards_of).reshape((-1,) + (1,) * (len(extent) - 1 - dim))
    return gain


def bell_draw(own_key, extent, scale, most, shards=(), kind=jnp.bfloat16):
    result = jax.random.normal(own_key, extent, jnp.float32) * scale
    if len(shards) > 0:
        result = shard_levels(own_key, extent, shards, -0.22, 0.18) * result
    return jnp.clip(result, min=-most, max=most).astype(kind)


def setup_inputs(seed: int = 0) -> dict:
    seeds = jax.random.split(jax.random.key(seed), 7)
    window = bell_draw(seeds[0], (ROWS_TM, ROWS_DP, WIN * GROUPS), 1.0, 6.0, ((0, 32), (1, 8)))
    link_ids = set_ends(jax.random.randint(seeds[1], (ROWS_TM, ROWS_DP), 0, GROUPS), jax.random.fold_in(seeds[1], 1), 0, GROUPS - 1).astype(jnp.int32)
    knot_ids = draw_knot_ids(jax.random.fold_in(seeds[6], 71), 0)
    lag_steps = draw_lag_steps(jax.random.fold_in(seeds[6], 71), 0)
    topology = set_ends((jax.random.randint(seeds[4], (GROUPS, GROUPS), 0, 2) < 1).astype(jnp.int32), jax.random.fold_in(seeds[4], 1), 0, 1)
    smooth = jnp.clip(jnp.exp(jax.random.uniform(seeds[5], (COEFS,), jnp.float32, math.log(200.0), math.log(6000.0))), 200.0, 6000.0)
    return {"window": window, "link_ids": link_ids, "knot_ids": knot_ids, "lag_steps": lag_steps, "topology": topology, "smooth": smooth}


RIDGE_TERM = 0.1

def regressors(frames_flat, link_rows, lag_steps, topology):
    samples = frames_flat.shape[0]
    frames = frames_flat.reshape(samples, WIN, GROUPS).astype(jnp.float32)
    picker = (jnp.arange(WIN)[None, :] == (WIN - 1 - lag_steps)[:, None]).astype(jnp.float32)
    lagged = jnp.einsum('lw,swg->slg', picker, frames)
    chosen = (link_rows[:, None] == jnp.arange(GROUPS)[None, :]).astype(jnp.float32)
    neighbour = jnp.dot(chosen, topology.astype(jnp.float32))
    design = (lagged * neighbour[:, None, :]).reshape(samples, NLAG * GROUPS).astype(jnp.bfloat16)
    target = lax.optimization_barrier(jnp.sum(frames[:, WIN - 1, :] * chosen, axis=1))
    return (design, target)

def reference(window, link_ids, knot_ids, lag_steps, topology, smooth):
    groups_all = N_DP * N_TM
    feats = WIN * GROUPS
    blocks = window.reshape(N_TM, RT, N_DP, N_DP, DEST, feats).transpose(3, 0, 1, 2, 4, 5).reshape(groups_all, RT * RD, feats)
    link_blocks = link_ids.reshape(N_TM, RT, N_DP, N_DP, DEST).transpose(3, 0, 1, 2, 4).reshape(groups_all, RT * RD)
    knot_blocks = knot_ids.reshape(N_TM, RT, N_DP, N_DP, DEST).transpose(3, 0, 1, 2, 4).reshape(groups_all, RT * RD)
    per_knot = RT * RD // KPD

    def assemble(inputs):
        frames, link_rows, knot_rows, index = inputs
        design, target = regressors(frames, link_rows, lag_steps, topology)
        design_wide = design.astype(jnp.float32)
        wanted = index * KPD + jnp.arange(KPD).astype(jnp.int32)
        weights = (knot_rows[:, None] == wanted[None, :]).astype(jnp.float32)
        grams = []
        moments = []
        for which in range(KPD):
            weighted = design_wide * weights[:, which:which + 1]
            grams.append(jnp.dot(weighted.T, design_wide, precision=lax.Precision.HIGHEST))
            moments.append(jnp.dot(weights[:, which] * target, design_wide, precision=lax.Precision.HIGHEST))
        return (jnp.stack(grams) / per_knot, jnp.stack(moments) / per_knot)
    indices = jnp.arange(groups_all).astype(jnp.int32)
    grams, moments = lax.map(assemble, (blocks, link_blocks, knot_blocks, indices))
    grams = grams.reshape(KNOTS, COEFS, COEFS)
    moments = moments.reshape(KNOTS, COEFS)
    positions = jnp.arange(KNOTS)
    neighbours = (positions > 0).astype(jnp.float32) + (positions < KNOTS - 1).astype(jnp.float32)
    identity = jnp.eye(COEFS, dtype=jnp.float32)
    penalty_diag = jnp.diag(smooth)

    def forward(carried, inputs):
        gram_block, moment_row, count = inputs
        system = gram_block + RIDGE_TERM * identity + jnp.diag(smooth * count) - smooth[:, None] * carried[:, :COEFS]
        forcing = moment_row + smooth * carried[:, COEFS]
        factor = jnp.linalg.cholesky(system)
        solved = jax.scipy.linalg.cho_solve((factor, True), jnp.concatenate([penalty_diag, forcing[:, None]], 1))
        return (solved, solved)
    start = jnp.zeros((COEFS, COEFS + 1), jnp.float32)
    _, stacked = lax.scan(forward, start, (grams, moments, neighbours))

    def backward(later, solved):
        current = solved[:, COEFS] + jnp.dot(solved[:, :COEFS], later, precision=lax.Precision.HIGHEST)
        return (current, current)
    _, solution = lax.scan(backward, jnp.zeros((COEFS,), jnp.float32), stacked, reverse=True)
    return solution * jnp.sqrt(jnp.float32(per_knot))
```

```python
import jax
import jax.numpy as jnp
from jax import lax
from jax.sharding import PartitionSpec as P

GROUPS = 64
NLAG = 4
WIN = 8
KPD = 2


RIDGE_TERM = 0.1


def from_behind(block, axis, distance):
    devices = range(lax.axis_size(axis))
    route = [(i - distance, i) for i in devices if i - distance in devices]
    return lax.ppermute(block, axis, route)


def regressors(frames_flat, link_rows, lag_steps, topology):
    samples = frames_flat.shape[0]
    frames = frames_flat.reshape(samples, WIN, GROUPS)
    picker = (
        lax.broadcasted_iota(jnp.int32, (NLAG, WIN), 1) == (WIN - 1 - lag_steps)[:, None]
    ).astype(jnp.bfloat16)
    lagged = jnp.einsum("lw,swg->slg", picker, frames, preferred_element_type=jnp.float32)
    chosen = (link_rows[:, None] == lax.broadcasted_iota(jnp.int32, (samples, GROUPS), 1)).astype(
        jnp.bfloat16
    )
    neighbour = jnp.dot(chosen, topology.astype(jnp.bfloat16), preferred_element_type=jnp.float32)
    design = (lagged * neighbour[:, None, :]).reshape(samples, NLAG * GROUPS).astype(jnp.bfloat16)
    target = jnp.sum(frames[:, WIN - 1, :].astype(jnp.float32) * chosen.astype(jnp.float32), axis=1)
    return (design, target)


def slot_terms(design, target, knot_slot, amount):

    def single(which):
        weight = (knot_slot == which).astype(jnp.bfloat16)
        weighted = design * weight[:, None]
        gram_part = jnp.einsum("sa,sb->ab", weighted, design, preferred_element_type=jnp.float32)
        scaled_target = (target * weight.astype(jnp.float32)).astype(jnp.bfloat16)
        moment_part = jnp.dot(scaled_target, design, preferred_element_type=jnp.float32)
        return jnp.concatenate([gram_part, moment_part[None, :]], 0)

    return lax.map(single, jnp.arange(amount))


def cholesky_solve(matrix, right_side):
    factor = jnp.linalg.cholesky(matrix)
    return jax.scipy.linalg.cho_solve((factor, True), right_side)


NS_TOL2 = 1e-6
NS_MAX_STEPS = 30


def solve_spd(matrix, right_side):
    size = matrix.shape[0]
    identity = jnp.eye(size, dtype=jnp.float32)
    inv_diag = 1.0 / jnp.diagonal(matrix)
    rows = jnp.sum(jnp.abs(matrix * inv_diag[:, None]), axis=1)
    upper = jnp.max(rows)
    lower = jnp.maximum(jnp.min(2.0 - rows), 0.0)
    start = jnp.diag(inv_diag * (2.0 / (upper + lower)))

    def residual(inverse):
        gap = identity - dense_dot(inverse, matrix)
        return gap, jnp.sum(gap * gap)

    def going(state):
        _, _, norm2, step = state
        return (step < NS_MAX_STEPS) & (norm2 > NS_TOL2) & jnp.isfinite(norm2)

    def refine(state):
        inverse, gap, _, step = state
        inverse = inverse + dense_dot(gap, inverse)
        gap, norm2 = residual(inverse)
        return (inverse, gap, norm2, step + 1)

    gap0, norm0 = residual(start)
    inverse, gap, norm2, _ = lax.while_loop(going, refine, (start, gap0, norm0, 0))
    inverse = inverse + dense_dot(gap, inverse)
    quick = dense_dot(inverse, right_side)
    return lax.cond(
        norm2 <= NS_TOL2,
        lambda: quick,
        lambda: cholesky_solve(matrix, right_side),
    )


def dense_dot(left_mat, right_mat):
    return jnp.dot(left_mat, right_mat, precision=lax.Precision.HIGHEST)


def body(window, link_ids, knot_ids, lag_steps, topology, smooth):
    n_dp = lax.axis_size("dp")
    n_tm = lax.axis_size("tm")
    device = lax.axis_index("dp") * n_tm + lax.axis_index("tm")
    devices = n_dp * n_tm
    columns = NLAG * GROUPS
    tm_rows, dp_rows, feats = window.shape
    samples = tm_rows * dp_rows
    per_knot = samples // KPD
    design, target = regressors(
        window.reshape(samples, feats), link_ids.reshape(samples), lag_steps, topology
    )
    knot_flat = knot_ids.reshape(samples)
    group_span = KPD * n_tm
    knot_slot = knot_flat // group_span * KPD + knot_flat % KPD
    packed = lax.psum_scatter(
        slot_terms(design, target, knot_slot, KPD * lax.axis_size("dp")),
        "dp",
        scatter_dimension=0,
        tiled=True,
    )
    grams = packed[:, :columns, :] / per_knot
    moments = packed[:, columns, :] / per_knot
    identity = jnp.eye(columns, dtype=jnp.float32)
    penalty_diag = jnp.diag(smooth)
    has_left = (device > 0).astype(jnp.float32)
    has_right = (device < devices - 1).astype(jnp.float32)

    def from_right(solved, stride):
        return from_behind(solved, ("dp", "tm"), -stride)

    def eliminate(system, left_coupling, right_coupling, forcing, left_solved, right_solved):
        left_term = dense_dot(left_coupling, left_solved)
        right_term = dense_dot(right_coupling, right_solved)
        new_system = system - left_term[:, columns : 2 * columns] - right_term[:, :columns]
        new_left = -left_term[:, :columns]
        new_right = -right_term[:, columns : 2 * columns]
        new_forcing = forcing - left_term[:, 2 * columns] - right_term[:, 2 * columns]
        return (new_system, new_left, new_right, new_forcing)

    even_system = grams[0] + RIDGE_TERM * identity + jnp.diag(smooth * (1.0 + has_left))
    even_solved = solve_spd(
        even_system,
        jnp.concatenate([-penalty_diag * has_left, -penalty_diag, moments[0][:, None]], 1),
    )
    next_solved = from_right(even_solved, 1)
    odd_system = grams[1] + RIDGE_TERM * identity + jnp.diag(smooth * (1.0 + has_right))
    system, left_coupling, right_coupling, forcing = eliminate(
        odd_system, -penalty_diag, -penalty_diag * has_right, moments[1], even_solved, next_solved
    )
    height = devices.bit_length() - 1
    for section in range(height):
        stride = 1 << section
        solved = solve_spd(
            system, jnp.concatenate([left_coupling, right_coupling, forcing[:, None]], 1)
        )
        left_in = from_behind(solved, ("dp", "tm"), stride)
        right_in = from_right(solved, stride)
        system, left_coupling, right_coupling, forcing = eliminate(
            system, left_coupling, right_coupling, forcing, left_in, right_in
        )
    solution = solve_spd(system, forcing[:, None])[:, 0]
    prior_odd = from_behind(solution, ("dp", "tm"), 1)
    even_knot = (
        even_solved[:, 2 * columns]
        - dense_dot(even_solved[:, :columns], prior_odd)
        - dense_dot(even_solved[:, columns : 2 * columns], solution)
    )
    return jnp.stack([even_knot, solution]) * jnp.sqrt(jnp.float32(per_knot))


def solution(mesh):
    return jax.shard_map(
        body,
        mesh=mesh,
        in_specs=(P("tm", "dp", None), P("tm", "dp"), P("tm", "dp"), P(), P(), P()),
        out_specs=P(("dp", "tm"), None),
        check_vma=False,
    )
```

```python
import jax
import jax.numpy as jnp
from jax import lax
from jax.sharding import PartitionSpec as P

GROUPS = 64
NLAG = 4
WIN = 8
KPD = 2


RIDGE_TERM = 0.1


def from_behind(block, axis, distance):
    devices = range(lax.axis_size(axis))
    route = [(i - distance, i) for i in devices if i - distance in devices]
    return lax.ppermute(block, axis, route)


def regressors(frames_flat, link_rows, lag_steps, topology):
    samples, feats = frames_flat.shape
    columns = NLAG * GROUPS
    source = lax.broadcasted_iota(jnp.int32, (feats, columns), 0)
    target_col = lax.broadcasted_iota(jnp.int32, (feats, columns), 1)
    lag_of_col = jnp.repeat(lag_steps, GROUPS, total_repeat_length=columns)
    wanted = (WIN - 1 - lag_of_col)[None, :] * GROUPS + target_col % GROUPS
    picker = (source == wanted).astype(jnp.bfloat16)
    lagged = jnp.dot(frames_flat, picker, preferred_element_type=jnp.float32)
    chosen = (link_rows[:, None] == lax.broadcasted_iota(jnp.int32, (samples, GROUPS), 1)).astype(
        jnp.bfloat16
    )
    neighbour = jnp.dot(chosen, topology.astype(jnp.bfloat16), preferred_element_type=jnp.float32)
    design = (lagged * jnp.tile(neighbour, (1, NLAG))).astype(jnp.bfloat16)
    latest = frames_flat[:, (WIN - 1) * GROUPS :].astype(jnp.float32)
    target = jnp.sum(latest * chosen.astype(jnp.float32), axis=1)
    return (design, target)


def slot_terms(design, target, knot_slot, amount):

    def single(which):
        weight = (knot_slot == which).astype(jnp.bfloat16)
        weighted = design * weight[:, None]
        gram_part = jnp.einsum("sa,sb->ab", weighted, design, preferred_element_type=jnp.float32)
        scaled_target = (target * weight.astype(jnp.float32)).astype(jnp.bfloat16)
        moment_part = jnp.dot(scaled_target, design, preferred_element_type=jnp.float32)
        return jnp.concatenate([gram_part, moment_part[None, :]], 0)

    return lax.map(single, jnp.arange(amount))


def cholesky_solve(matrix, right_side):
    factor = jnp.linalg.cholesky(matrix)
    return jax.scipy.linalg.cho_solve((factor, True), right_side)


NS_TOL2 = 1e-6
NS_MAX_STEPS = 30


def solve_spd(matrix, right_side):
    size = matrix.shape[0]
    identity = jnp.eye(size, dtype=jnp.float32)
    inv_diag = 1.0 / jnp.diagonal(matrix)
    rows = jnp.sum(jnp.abs(matrix * inv_diag[:, None]), axis=1)
    upper = jnp.max(rows)
    lower = jnp.maximum(jnp.min(2.0 - rows), 0.0)
    start = jnp.diag(inv_diag * (2.0 / (upper + lower)))

    def residual(inverse):
        gap = identity - dense_dot(inverse, matrix)
        return gap, jnp.sum(gap * gap)

    def going(state):
        _, _, norm2, step = state
        return (step < NS_MAX_STEPS) & (norm2 > NS_TOL2) & jnp.isfinite(norm2)

    def refine(state):
        inverse, gap, _, step = state
        inverse = inverse + dense_dot(gap, inverse)
        gap, norm2 = residual(inverse)
        return (inverse, gap, norm2, step + 1)

    gap0, norm0 = residual(start)
    inverse, gap, norm2, _ = lax.while_loop(going, refine, (start, gap0, norm0, 0))
    inverse = inverse + dense_dot(gap, inverse)
    quick = dense_dot(inverse, right_side)
    return lax.cond(
        norm2 <= NS_TOL2,
        lambda: quick,
        lambda: cholesky_solve(matrix, right_side),
    )


def dense_dot(left_mat, right_mat):
    return jnp.dot(left_mat, right_mat, precision=lax.Precision.HIGHEST)


def body(window, link_ids, knot_ids, lag_steps, topology, smooth):
    n_dp = lax.axis_size("dp")
    n_tm = lax.axis_size("tm")
    device = lax.axis_index("dp") * n_tm + lax.axis_index("tm")
    devices = n_dp * n_tm
    columns = NLAG * GROUPS
    tm_rows, dp_rows, feats = window.shape
    samples = tm_rows * dp_rows
    per_knot = samples // KPD
    design, target = regressors(
        window.reshape(samples, feats), link_ids.reshape(samples), lag_steps, topology
    )
    dest = dp_rows // n_dp
    by_owner = design.reshape(tm_rows, n_dp, dest, columns).transpose(1, 0, 2, 3)
    parity = (knot_ids.reshape(samples) % KPD).astype(jnp.float32)
    side = jnp.stack([target, parity], 0).reshape(2, tm_rows, n_dp, dest).transpose(2, 0, 1, 3)
    got = lax.all_to_all(
        by_owner.reshape(n_dp, tm_rows * dest, columns), "dp", 0, 0, tiled=True
    ).reshape(samples, columns)
    got_side = lax.all_to_all(
        side.reshape(n_dp, 2, tm_rows * dest), "dp", 0, 0, tiled=True
    )
    got_target = got_side[:, 0, :].reshape(samples)
    got_parity = got_side[:, 1, :].reshape(samples)
    grams = []
    moments = []
    for which in range(KPD):
        weight = (got_parity == which).astype(jnp.bfloat16)
        weighted = got * weight[:, None]
        grams.append(
            jnp.einsum("sa,sb->ab", weighted, got, preferred_element_type=jnp.float32) / per_knot
        )
        scaled_target = (got_target * weight.astype(jnp.float32)).astype(jnp.bfloat16)
        moments.append(jnp.dot(scaled_target, got, preferred_element_type=jnp.float32) / per_knot)
    identity = jnp.eye(columns, dtype=jnp.float32)
    penalty_diag = jnp.diag(smooth)
    has_left = (device > 0).astype(jnp.float32)
    has_right = (device < devices - 1).astype(jnp.float32)

    def from_right(solved, stride):
        return from_behind(solved, ("dp", "tm"), -stride)

    def eliminate(system, left_coupling, right_coupling, forcing, left_solved, right_solved):
        left_term = dense_dot(left_coupling, left_solved)
        right_term = dense_dot(right_coupling, right_solved)
        new_system = system - left_term[:, columns : 2 * columns] - right_term[:, :columns]
        new_left = -left_term[:, :columns]
        new_right = -right_term[:, columns : 2 * columns]
        new_forcing = forcing - left_term[:, 2 * columns] - right_term[:, 2 * columns]
        return (new_system, new_left, new_right, new_forcing)

    even_system = grams[0] + RIDGE_TERM * identity + jnp.diag(smooth * (1.0 + has_left))
    even_solved = solve_spd(
        even_system,
        jnp.concatenate([-penalty_diag * has_left, -penalty_diag, moments[0][:, None]], 1),
    )
    next_solved = from_right(even_solved, 1)
    odd_system = grams[1] + RIDGE_TERM * identity + jnp.diag(smooth * (1.0 + has_right))
    system, left_coupling, right_coupling, forcing = eliminate(
        odd_system, -penalty_diag, -penalty_diag * has_right, moments[1], even_solved, next_solved
    )
    height = devices.bit_length() - 1
    for section in range(height):
        stride = 1 << section
        solved = solve_spd(
            system, jnp.concatenate([left_coupling, right_coupling, forcing[:, None]], 1)
        )
        left_in = from_behind(solved, ("dp", "tm"), stride)
        right_in = from_right(solved, stride)
        system, left_coupling, right_coupling, forcing = eliminate(
            system, left_coupling, right_coupling, forcing, left_in, right_in
        )
    solution = solve_spd(system, forcing[:, None])[:, 0]
    prior_odd = from_behind(solution, ("dp", "tm"), 1)
    even_knot = (
        even_solved[:, 2 * columns]
        - dense_dot(even_solved[:, :columns], prior_odd)
        - dense_dot(even_solved[:, columns : 2 * columns], solution)
    )
    return jnp.stack([even_knot, solution]) * jnp.sqrt(jnp.float32(per_knot))


def solution(mesh):
    return jax.shard_map(
        body,
        mesh=mesh,
        in_specs=(P("tm", "dp", None), P("tm", "dp"), P("tm", "dp"), P(), P(), P()),
        out_specs=P(("dp", "tm"), None),
        check_vma=False,
    )
```

```python
import jax
import jax.numpy as jnp
from jax import lax
from jax.sharding import PartitionSpec as P

GROUPS = 64
NLAG = 4
WIN = 8
KPD = 2


RIDGE_TERM = 0.1


def from_behind(block, axis, distance):
    devices = range(lax.axis_size(axis))
    route = [(i - distance, i) for i in devices if i - distance in devices]
    return lax.ppermute(block, axis, route)


def regressors(frames_flat, link_rows, lag_steps, topology):
    samples, feats = frames_flat.shape
    columns = NLAG * GROUPS
    source = lax.broadcasted_iota(jnp.int32, (feats, columns), 0)
    target_col = lax.broadcasted_iota(jnp.int32, (feats, columns), 1)
    lag_of_col = jnp.repeat(lag_steps, GROUPS, total_repeat_length=columns)
    wanted = (WIN - 1 - lag_of_col)[None, :] * GROUPS + target_col % GROUPS
    picker = (source == wanted).astype(jnp.bfloat16)
    lagged = jnp.dot(frames_flat, picker, preferred_element_type=jnp.float32)
    chosen = (link_rows[:, None] == lax.broadcasted_iota(jnp.int32, (samples, GROUPS), 1)).astype(
        jnp.bfloat16
    )
    neighbour = jnp.dot(chosen, topology.astype(jnp.bfloat16), preferred_element_type=jnp.float32)
    design = (lagged * jnp.tile(neighbour, (1, NLAG))).astype(jnp.bfloat16)
    latest = frames_flat[:, (WIN - 1) * GROUPS :].astype(jnp.float32)
    target = jnp.sum(latest * chosen.astype(jnp.float32), axis=1)
    return (design, target)


def slot_terms(design, target, knot_slot, amount):

    def single(which):
        weight = (knot_slot == which).astype(jnp.bfloat16)
        weighted = design * weight[:, None]
        gram_part = jnp.einsum("sa,sb->ab", weighted, design, preferred_element_type=jnp.float32)
        scaled_target = (target * weight.astype(jnp.float32)).astype(jnp.bfloat16)
        moment_part = jnp.dot(scaled_target, design, preferred_element_type=jnp.float32)
        return jnp.concatenate([gram_part, moment_part[None, :]], 0)

    return lax.map(single, jnp.arange(amount))


def cholesky_solve(matrix, right_side):
    factor = jnp.linalg.cholesky(matrix)
    return jax.scipy.linalg.cho_solve((factor, True), right_side)


NS_TOL2 = 1e-6
NS_MAX_STEPS = 30


def spd_inverse(matrix):
    size = matrix.shape[0]
    identity = jnp.eye(size, dtype=jnp.float32)
    inv_diag = 1.0 / jnp.sum(matrix * identity, axis=1)
    rows = jnp.sum(jnp.abs(matrix * inv_diag[:, None]), axis=1)
    upper = jnp.max(rows)
    lower = jnp.maximum(jnp.min(2.0 - rows), 0.0)
    start = identity * (inv_diag * (2.0 / (upper + lower)))[:, None]

    def residual(inverse):
        gap = identity - dense_dot(inverse, matrix)
        return gap, jnp.sum(gap * gap)

    def going(state):
        _, _, norm2, step = state
        return (step < NS_MAX_STEPS) & (norm2 > NS_TOL2) & jnp.isfinite(norm2)

    def refine(state):
        inverse, gap, _, step = state
        inverse = inverse + dense_dot(gap, inverse)
        gap, norm2 = residual(inverse)
        return (inverse, gap, norm2, step + 1)

    gap0, norm0 = residual(start)
    inverse, gap, norm2, _ = lax.while_loop(going, refine, (start, gap0, norm0, 0))
    return lax.cond(
        norm2 <= NS_TOL2,
        lambda: inverse + dense_dot(gap, inverse),
        lambda: cholesky_solve(matrix, identity),
    )


def solve_spd(matrix, right_side):
    return dense_dot(spd_inverse(matrix), right_side)


def dense_dot(left_mat, right_mat):
    return jnp.dot(left_mat, right_mat, precision=lax.Precision.HIGHEST)


def body(window, link_ids, knot_ids, lag_steps, topology, smooth):
    n_dp = lax.axis_size("dp")
    n_tm = lax.axis_size("tm")
    device = lax.axis_index("dp") * n_tm + lax.axis_index("tm")
    devices = n_dp * n_tm
    columns = NLAG * GROUPS
    tm_rows, dp_rows, feats = window.shape
    samples = tm_rows * dp_rows
    per_knot = samples // KPD
    design, target = regressors(
        window.reshape(samples, feats), link_ids.reshape(samples), lag_steps, topology
    )
    dest = dp_rows // n_dp
    by_owner = design.reshape(tm_rows, n_dp, dest, columns).transpose(1, 0, 2, 3)
    parity = (knot_ids.reshape(samples) % KPD).astype(jnp.float32)
    side = jnp.stack([target, parity], 0).reshape(2, tm_rows, n_dp, dest).transpose(2, 0, 1, 3)
    got = lax.all_to_all(
        by_owner.reshape(n_dp, tm_rows * dest, columns), "dp", 0, 0, tiled=True
    ).reshape(samples, columns)
    got_side = lax.all_to_all(
        side.reshape(n_dp, 2, tm_rows * dest), "dp", 0, 0, tiled=True
    )
    got_target = got_side[:, 0, :].reshape(samples)
    got_parity = got_side[:, 1, :].reshape(samples)
    grams = []
    moments = []
    for which in range(KPD):
        weight = (got_parity == which).astype(jnp.bfloat16)
        weighted = got * weight[:, None]
        grams.append(
            jnp.einsum("sa,sb->ab", weighted, got, preferred_element_type=jnp.float32) / per_knot
        )
        scaled_target = (got_target * weight.astype(jnp.float32)).astype(jnp.bfloat16)
        moments.append(jnp.dot(scaled_target, got, preferred_element_type=jnp.float32) / per_knot)
    identity = jnp.eye(columns, dtype=jnp.float32)
    penalty_diag = jnp.diag(smooth)
    has_left = (device > 0).astype(jnp.float32)
    has_right = (device < devices - 1).astype(jnp.float32)

    def from_right(solved, stride):
        return from_behind(solved, ("dp", "tm"), -stride)

    def eliminate(system, left_coupling, right_coupling, forcing, from_left, from_right_side):
        first_left, rest_left = from_left
        first_right, rest_right = from_right_side
        new_system = (
            system - dense_dot(left_coupling, first_left) - dense_dot(right_coupling, first_right)
        )
        left_term = dense_dot(left_coupling, rest_left)
        right_term = dense_dot(right_coupling, rest_right)
        new_left = -left_term[:, :columns]
        new_right = -right_term[:, :columns]
        new_forcing = forcing - left_term[:, columns] - right_term[:, columns]
        return (new_system, new_left, new_right, new_forcing)

    def split_solve(system, left_coupling, right_coupling, forcing):
        inverse = spd_inverse(system)
        y_left = dense_dot(inverse, left_coupling)
        y_right = dense_dot(inverse, right_coupling)
        y_force = dense_dot(inverse, forcing[:, None])
        return y_left, y_right, y_force

    def exchange(y_left, y_right, y_force, stride):
        first_left = from_behind(y_right, ("dp", "tm"), stride)
        first_right = from_right(y_left, stride)
        rest_left = from_behind(jnp.concatenate([y_left, y_force], 1), ("dp", "tm"), stride)
        rest_right = from_right(jnp.concatenate([y_right, y_force], 1), stride)
        return (first_left, rest_left), (first_right, rest_right)

    even_system = grams[0] + RIDGE_TERM * identity + jnp.diag(smooth * (1.0 + has_left))
    even_left, even_right, even_force = split_solve(
        even_system, -penalty_diag * has_left, -penalty_diag, moments[0]
    )
    _, next_even = exchange(even_left, even_right, even_force, 1)
    odd_system = grams[1] + RIDGE_TERM * identity + jnp.diag(smooth * (1.0 + has_right))
    own_even = (even_right, jnp.concatenate([even_left, even_force], 1))
    system, left_coupling, right_coupling, forcing = eliminate(
        odd_system, -penalty_diag, -penalty_diag * has_right, moments[1], own_even, next_even
    )
    height = devices.bit_length() - 1
    for section in range(height):
        stride = 1 << section
        y_left, y_right, y_force = split_solve(system, left_coupling, right_coupling, forcing)
        left_in, right_in = exchange(y_left, y_right, y_force, stride)
        system, left_coupling, right_coupling, forcing = eliminate(
            system, left_coupling, right_coupling, forcing, left_in, right_in
        )
    solution = solve_spd(system, forcing[:, None])[:, 0]
    prior_odd = from_behind(solution, ("dp", "tm"), 1)
    even_knot = (
        even_force[:, 0]
        - dense_dot(even_left, prior_odd)
        - dense_dot(even_right, solution)
    )
    return jnp.stack([even_knot, solution]) * jnp.sqrt(jnp.float32(per_knot))


def solution(mesh):
    return jax.shard_map(
        body,
        mesh=mesh,
        in_specs=(P("tm", "dp", None), P("tm", "dp"), P("tm", "dp"), P(), P(), P()),
        out_specs=P(("dp", "tm"), None),
        check_vma=False,
    )
```

```python
import jax
import jax.numpy as jnp
from jax import lax
from jax.sharding import PartitionSpec as P

GROUPS = 64
NLAG = 4
WIN = 8
KPD = 2


RIDGE_TERM = 0.1


def from_behind(block, axis, distance):
    devices = range(lax.axis_size(axis))
    route = [(i - distance, i) for i in devices if i - distance in devices]
    return lax.ppermute(block, axis, route)


def regressors(frames_flat, link_rows, lag_steps, topology):
    samples, feats = frames_flat.shape
    columns = NLAG * GROUPS
    source = lax.broadcasted_iota(jnp.int32, (feats, columns), 0)
    target_col = lax.broadcasted_iota(jnp.int32, (feats, columns), 1)
    lag_of_col = jnp.repeat(lag_steps, GROUPS, total_repeat_length=columns)
    wanted = (WIN - 1 - lag_of_col)[None, :] * GROUPS + target_col % GROUPS
    picker = (source == wanted).astype(jnp.bfloat16)
    lagged = jnp.dot(frames_flat, picker, preferred_element_type=jnp.float32)
    chosen = (link_rows[:, None] == lax.broadcasted_iota(jnp.int32, (samples, GROUPS), 1)).astype(
        jnp.bfloat16
    )
    neighbour = jnp.dot(chosen, topology.astype(jnp.bfloat16), preferred_element_type=jnp.float32)
    design = (lagged * jnp.tile(neighbour, (1, NLAG))).astype(jnp.bfloat16)
    latest = frames_flat[:, (WIN - 1) * GROUPS :].astype(jnp.float32)
    target = jnp.sum(latest * chosen.astype(jnp.float32), axis=1)
    return (design, target)


NS_TOL2 = 1e-6
NS_FIXED_STEPS = 3
NS_MAX_STEPS = 40


def spd_inverse(matrix):
    size = matrix.shape[0]
    identity = jnp.eye(size, dtype=jnp.float32)
    inv_diag = 1.0 / jnp.sum(matrix * identity, axis=1)
    rows = jnp.sum(jnp.abs(matrix * inv_diag[:, None]), axis=1)
    upper = jnp.max(rows)
    lower = jnp.maximum(jnp.min(2.0 - rows), 0.0)
    inverse = identity * (inv_diag * (2.0 / (upper + lower)))[:, None]
    for _ in range(NS_FIXED_STEPS):
        inverse = inverse + dense_dot(identity - dense_dot(inverse, matrix), inverse)

    def residual(inverse):
        gap = identity - dense_dot(inverse, matrix)
        return gap, jnp.sum(gap * gap)

    def going(state):
        _, _, norm2, prev2, _, _, best2, step = state
        stalled = (norm2 < 1e-2) & (norm2 > 0.25 * prev2)
        return (step < NS_MAX_STEPS) & (best2 > NS_TOL2) & jnp.isfinite(norm2) & ~stalled

    def refine(state):
        inverse, gap, norm2, _, best, best_gap, best2, step = state
        new_inverse = inverse + dense_dot(gap, inverse)
        new_gap, new2 = residual(new_inverse)
        better = new2 < best2
        best = jnp.where(better, new_inverse, best)
        best_gap = jnp.where(better, new_gap, best_gap)
        best2 = jnp.where(better, new2, best2)
        return (new_inverse, new_gap, new2, norm2, best, best_gap, best2, step + 1)

    gap, norm2 = residual(inverse)
    state = (inverse, gap, norm2, jnp.float32(jnp.inf), inverse, gap, norm2, 0)
    _, _, _, _, best, best_gap, _, _ = lax.while_loop(going, refine, state)
    return best + dense_dot(best_gap, best)


def solve_spd(matrix, right_side):
    return dense_dot(spd_inverse(matrix), right_side)


def dense_dot(left_mat, right_mat):
    return jnp.dot(left_mat, right_mat, precision=lax.Precision.HIGHEST)


def body(window, link_ids, knot_ids, lag_steps, topology, smooth):
    n_dp = lax.axis_size("dp")
    n_tm = lax.axis_size("tm")
    device = lax.axis_index("dp") * n_tm + lax.axis_index("tm")
    devices = n_dp * n_tm
    columns = NLAG * GROUPS
    tm_rows, dp_rows, feats = window.shape
    samples = tm_rows * dp_rows
    per_knot = samples // KPD
    design, target = regressors(
        window.reshape(samples, feats), link_ids.reshape(samples), lag_steps, topology
    )
    dest = dp_rows // n_dp
    by_owner = design.reshape(tm_rows, n_dp, dest, columns).transpose(1, 0, 2, 3)
    parity = (knot_ids.reshape(samples) % KPD).astype(jnp.float32)
    side = jnp.stack([target, parity], 0).reshape(2, tm_rows, n_dp, dest).transpose(2, 0, 1, 3)
    got = lax.all_to_all(
        by_owner.reshape(n_dp, tm_rows * dest, columns), "dp", 0, 0, tiled=True
    ).reshape(samples, columns)
    got_side = lax.all_to_all(
        side.reshape(n_dp, 2, tm_rows * dest), "dp", 0, 0, tiled=True
    )
    got_target = got_side[:, 0, :].reshape(samples)
    got_parity = got_side[:, 1, :].reshape(samples)
    grams = []
    moments = []
    for which in range(KPD):
        weight = (got_parity == which).astype(jnp.bfloat16)
        weighted = got * weight[:, None]
        grams.append(
            jnp.einsum("sa,sb->ab", weighted, got, preferred_element_type=jnp.float32) / per_knot
        )
        scaled_target = (got_target * weight.astype(jnp.float32)).astype(jnp.bfloat16)
        moments.append(jnp.dot(scaled_target, got, preferred_element_type=jnp.float32) / per_knot)
    identity = jnp.eye(columns, dtype=jnp.float32)
    penalty_diag = jnp.diag(smooth)
    has_left = (device > 0).astype(jnp.float32)
    has_right = (device < devices - 1).astype(jnp.float32)

    def from_right(solved, stride):
        return from_behind(solved, ("dp", "tm"), -stride)

    def eliminate(system, left_coupling, right_coupling, forcing, from_left, from_right_side):
        first_left, rest_left = from_left
        first_right, rest_right = from_right_side
        new_system = (
            system - dense_dot(left_coupling, first_left) - dense_dot(right_coupling, first_right)
        )
        left_term = dense_dot(left_coupling, rest_left)
        right_term = dense_dot(right_coupling, rest_right)
        new_left = -left_term[:, :columns]
        new_right = -right_term[:, :columns]
        new_forcing = forcing - left_term[:, columns] - right_term[:, columns]
        return (new_system, new_left, new_right, new_forcing)

    def split_solve(system, left_coupling, right_coupling, forcing):
        inverse = spd_inverse(system)
        y_left = dense_dot(inverse, left_coupling)
        y_right = dense_dot(inverse, right_coupling)
        y_force = dense_dot(inverse, forcing[:, None])
        return y_left, y_right, y_force

    def exchange(y_left, y_right, y_force, stride):
        first_left = from_behind(y_right, ("dp", "tm"), stride)
        first_right = from_right(y_left, stride)
        rest_left = from_behind(jnp.concatenate([y_left, y_force], 1), ("dp", "tm"), stride)
        rest_right = from_right(jnp.concatenate([y_right, y_force], 1), stride)
        return (first_left, rest_left), (first_right, rest_right)

    even_system = grams[0] + RIDGE_TERM * identity + jnp.diag(smooth * (1.0 + has_left))
    even_left, even_right, even_force = split_solve(
        even_system, -penalty_diag * has_left, -penalty_diag, moments[0]
    )
    _, next_even = exchange(even_left, even_right, even_force, 1)
    odd_system = grams[1] + RIDGE_TERM * identity + jnp.diag(smooth * (1.0 + has_right))
    own_even = (even_right, jnp.concatenate([even_left, even_force], 1))
    system, left_coupling, right_coupling, forcing = eliminate(
        odd_system, -penalty_diag, -penalty_diag * has_right, moments[1], own_even, next_even
    )
    height = devices.bit_length() - 1
    for section in range(height):
        stride = 1 << section
        y_left, y_right, y_force = split_solve(system, left_coupling, right_coupling, forcing)
        left_in, right_in = exchange(y_left, y_right, y_force, stride)
        system, left_coupling, right_coupling, forcing = eliminate(
            system, left_coupling, right_coupling, forcing, left_in, right_in
        )
    solution = solve_spd(system, forcing[:, None])[:, 0]
    prior_odd = from_behind(solution, ("dp", "tm"), 1)
    even_knot = (
        even_force[:, 0]
        - dense_dot(even_left, prior_odd)
        - dense_dot(even_right, solution)
    )
    return jnp.stack([even_knot, solution]) * jnp.sqrt(jnp.float32(per_knot))


def solution(mesh):
    return jax.shard_map(
        body,
        mesh=mesh,
        in_specs=(P("tm", "dp", None), P("tm", "dp"), P("tm", "dp"), P(), P(), P()),
        out_specs=P(("dp", "tm"), None),
        check_vma=False,
    )
```

```python
import jax
import jax.numpy as jnp
from jax import lax
from jax.sharding import PartitionSpec as P

GROUPS = 64
NLAG = 4
WIN = 8
KPD = 2


RIDGE_TERM = 0.1


def from_behind(block, axis, distance):
    devices = range(lax.axis_size(axis))
    route = [(i - distance, i) for i in devices if i - distance in devices]
    return lax.ppermute(block, axis, route)


def regressors(frames_flat, link_rows, lag_steps, topology):
    samples, feats = frames_flat.shape
    columns = NLAG * GROUPS
    source = lax.broadcasted_iota(jnp.int32, (feats, columns), 0)
    target_col = lax.broadcasted_iota(jnp.int32, (feats, columns), 1)
    lag_of_col = jnp.repeat(lag_steps, GROUPS, total_repeat_length=columns)
    wanted = (WIN - 1 - lag_of_col)[None, :] * GROUPS + target_col % GROUPS
    picker = (source == wanted).astype(jnp.bfloat16)
    lagged = jnp.dot(frames_flat, picker, preferred_element_type=jnp.float32)
    chosen = (link_rows[:, None] == lax.broadcasted_iota(jnp.int32, (samples, GROUPS), 1)).astype(
        jnp.bfloat16
    )
    neighbour = jnp.dot(chosen, topology.astype(jnp.bfloat16), preferred_element_type=jnp.float32)
    design = (lagged * jnp.tile(neighbour, (1, NLAG))).astype(jnp.bfloat16)
    latest = frames_flat[:, (WIN - 1) * GROUPS :].astype(jnp.float32)
    target = jnp.sum(latest * chosen.astype(jnp.float32), axis=1)
    return (design, target)


NS_TOL2 = 1e-6
NS_FIXED_STEPS = 3
NS_MAX_STEPS = 40


def spd_inverse(matrix):
    size = matrix.shape[0]
    identity = jnp.eye(size, dtype=jnp.float32)
    inv_diag = 1.0 / jnp.sum(matrix * identity, axis=1)
    rows = jnp.sum(jnp.abs(matrix * inv_diag[:, None]), axis=1)
    upper = jnp.max(rows)
    lower = jnp.maximum(jnp.min(2.0 - rows), 0.0)
    inverse = identity * (inv_diag * (2.0 / (upper + lower)))[:, None]
    for _ in range(NS_FIXED_STEPS):
        inverse = inverse + dense_dot(identity - dense_dot(inverse, matrix), inverse)

    def residual(inverse):
        gap = identity - dense_dot(inverse, matrix)
        return gap, jnp.sum(gap * gap)

    def going(state):
        _, _, norm2, prev2, _, _, best2, step = state
        stalled = (norm2 < 1e-2) & (norm2 > 0.25 * prev2)
        return (step < NS_MAX_STEPS) & (best2 > NS_TOL2) & jnp.isfinite(norm2) & ~stalled

    def refine(state):
        inverse, gap, norm2, _, best, best_gap, best2, step = state
        new_inverse = inverse + dense_dot(gap, inverse)
        new_gap, new2 = residual(new_inverse)
        better = new2 < best2
        best = jnp.where(better, new_inverse, best)
        best_gap = jnp.where(better, new_gap, best_gap)
        best2 = jnp.where(better, new2, best2)
        return (new_inverse, new_gap, new2, norm2, best, best_gap, best2, step + 1)

    gap, norm2 = residual(inverse)
    state = (inverse, gap, norm2, jnp.float32(jnp.inf), inverse, gap, norm2, 0)
    _, _, _, _, best, best_gap, _, _ = lax.while_loop(going, refine, state)
    return best + dense_dot(best_gap, best)


def solve_spd(matrix, right_side):
    return dense_dot(spd_inverse(matrix), right_side)


def dense_dot(left_mat, right_mat):
    return jnp.dot(left_mat, right_mat, precision=lax.Precision.HIGHEST)


def body(window, link_ids, knot_ids, lag_steps, topology, smooth):
    n_dp = lax.axis_size("dp")
    n_tm = lax.axis_size("tm")
    device = lax.axis_index("dp") * n_tm + lax.axis_index("tm")
    devices = n_dp * n_tm
    columns = NLAG * GROUPS
    tm_rows, dp_rows, feats = window.shape
    samples = tm_rows * dp_rows
    per_knot = samples // KPD
    design, target = regressors(
        window.reshape(samples, feats), link_ids.reshape(samples), lag_steps, topology
    )
    dest = dp_rows // n_dp
    by_owner = design.reshape(tm_rows, n_dp, dest, columns).transpose(1, 0, 2, 3)
    parity = (knot_ids.reshape(samples) % KPD).astype(jnp.float32)
    side = jnp.stack([target, parity], 0).reshape(2, tm_rows, n_dp, dest).transpose(2, 0, 1, 3)
    per_owner = tm_rows * dest
    side = side.reshape(n_dp, 2, per_owner).astype(jnp.bfloat16)
    if per_owner == columns:
        parcel = jnp.concatenate([by_owner.reshape(n_dp, per_owner, columns), side], 1)
        got_all = lax.all_to_all(parcel, "dp", 0, 0, tiled=True)
        got = got_all[:, :per_owner, :].reshape(samples, columns)
        got_side = got_all[:, per_owner:, :].astype(jnp.float32)
    else:
        got = lax.all_to_all(
            by_owner.reshape(n_dp, per_owner, columns), "dp", 0, 0, tiled=True
        ).reshape(samples, columns)
        got_side = lax.all_to_all(side, "dp", 0, 0, tiled=True).astype(jnp.float32)
    got_target = got_side[:, 0, :].reshape(samples)
    got_parity = got_side[:, 1, :].reshape(samples)
    grams = []
    moments = []
    for which in range(KPD):
        weight = (got_parity == which).astype(jnp.bfloat16)
        weighted = got * weight[:, None]
        grams.append(
            jnp.einsum("sa,sb->ab", weighted, got, preferred_element_type=jnp.float32) / per_knot
        )
        scaled_target = (got_target * weight.astype(jnp.float32)).astype(jnp.bfloat16)
        moments.append(jnp.dot(scaled_target, got, preferred_element_type=jnp.float32) / per_knot)
    identity = jnp.eye(columns, dtype=jnp.float32)
    penalty_diag = jnp.diag(smooth)
    has_left = (device > 0).astype(jnp.float32)
    has_right = (device < devices - 1).astype(jnp.float32)

    def from_right(solved, stride):
        return from_behind(solved, ("dp", "tm"), -stride)

    def eliminate(system, left_coupling, right_coupling, forcing, from_left, from_right_side):
        first_left, rest_left = from_left
        first_right, rest_right = from_right_side
        new_system = (
            system - dense_dot(left_coupling, first_left) - dense_dot(right_coupling, first_right)
        )
        left_term = dense_dot(left_coupling, rest_left)
        right_term = dense_dot(right_coupling, rest_right)
        new_left = -left_term[:, :columns]
        new_right = -right_term[:, :columns]
        new_forcing = forcing - left_term[:, columns] - right_term[:, columns]
        return (new_system, new_left, new_right, new_forcing)

    def split_solve(system, left_coupling, right_coupling, forcing):
        inverse = spd_inverse(system)
        y_left = dense_dot(inverse, left_coupling)
        y_right = dense_dot(inverse, right_coupling)
        y_force = dense_dot(inverse, forcing[:, None])
        return y_left, y_right, y_force

    def exchange(y_left, y_right, y_force, stride):
        first_left = from_behind(y_right, ("dp", "tm"), stride)
        first_right = from_right(y_left, stride)
        rest_left = from_behind(jnp.concatenate([y_left, y_force], 1), ("dp", "tm"), stride)
        rest_right = from_right(jnp.concatenate([y_right, y_force], 1), stride)
        return (first_left, rest_left), (first_right, rest_right)

    even_system = grams[0] + RIDGE_TERM * identity + jnp.diag(smooth * (1.0 + has_left))
    even_left, even_right, even_force = split_solve(
        even_system, -penalty_diag * has_left, -penalty_diag, moments[0]
    )
    _, next_even = exchange(even_left, even_right, even_force, 1)
    odd_system = grams[1] + RIDGE_TERM * identity + jnp.diag(smooth * (1.0 + has_right))
    own_even = (even_right, jnp.concatenate([even_left, even_force], 1))
    system, left_coupling, right_coupling, forcing = eliminate(
        odd_system, -penalty_diag, -penalty_diag * has_right, moments[1], own_even, next_even
    )
    height = devices.bit_length() - 1
    for section in range(height):
        stride = 1 << section
        y_left, y_right, y_force = split_solve(system, left_coupling, right_coupling, forcing)
        left_in, right_in = exchange(y_left, y_right, y_force, stride)
        system, left_coupling, right_coupling, forcing = eliminate(
            system, left_coupling, right_coupling, forcing, left_in, right_in
        )
    solution = solve_spd(system, forcing[:, None])[:, 0]
    prior_odd = from_behind(solution, ("dp", "tm"), 1)
    even_knot = (
        even_force[:, 0]
        - dense_dot(even_left, prior_odd)
        - dense_dot(even_right, solution)
    )
    return jnp.stack([even_knot, solution]) * jnp.sqrt(jnp.float32(per_knot))


def solution(mesh):
    return jax.shard_map(
        body,
        mesh=mesh,
        in_specs=(P("tm", "dp", None), P("tm", "dp"), P("tm", "dp"), P(), P(), P()),
        out_specs=P(("dp", "tm"), None),
        check_vma=False,
    )
```

```python
import jax
import jax.numpy as jnp
from jax import lax
from jax.sharding import PartitionSpec as P

GROUPS = 64
NLAG = 4
WIN = 8
KPD = 2


RIDGE_TERM = 0.1


def from_behind(block, axis, distance):
    devices = range(lax.axis_size(axis))
    route = [(i - distance, i) for i in devices if i - distance in devices]
    return lax.ppermute(block, axis, route)


def regressors(frames_flat, link_rows, lag_steps, topology):
    samples, feats = frames_flat.shape
    columns = NLAG * GROUPS
    source = lax.broadcasted_iota(jnp.int32, (feats, columns), 0)
    target_col = lax.broadcasted_iota(jnp.int32, (feats, columns), 1)
    lag_of_col = jnp.repeat(lag_steps, GROUPS, total_repeat_length=columns)
    wanted = (WIN - 1 - lag_of_col)[None, :] * GROUPS + target_col % GROUPS
    picker = (source == wanted).astype(jnp.bfloat16)
    lagged = jnp.dot(frames_flat, picker, preferred_element_type=jnp.float32)
    chosen = (link_rows[:, None] == lax.broadcasted_iota(jnp.int32, (samples, GROUPS), 1)).astype(
        jnp.bfloat16
    )
    neighbour = jnp.dot(chosen, topology.astype(jnp.bfloat16), preferred_element_type=jnp.float32)
    design = (lagged * jnp.tile(neighbour, (1, NLAG))).astype(jnp.bfloat16)
    latest = frames_flat[:, (WIN - 1) * GROUPS :].astype(jnp.float32)
    target = jnp.sum(latest * chosen.astype(jnp.float32), axis=1)
    return (design, target)


NS_TOL2 = 1e-6
NS_FIXED_STEPS = 3
NS_MAX_STEPS = 40


def spd_inverse(matrix):
    size = matrix.shape[0]
    identity = jnp.eye(size, dtype=jnp.float32)
    inv_diag = 1.0 / jnp.sum(matrix * identity, axis=1)
    rows = jnp.sum(jnp.abs(matrix * inv_diag[:, None]), axis=1)
    upper = jnp.max(rows)
    lower = jnp.maximum(jnp.min(2.0 - rows), 0.0)
    inverse = identity * (inv_diag * (2.0 / (upper + lower)))[:, None]
    for _ in range(NS_FIXED_STEPS):
        inverse = inverse + dense_dot(identity - dense_dot(inverse, matrix), inverse)

    def residual(inverse):
        gap = identity - dense_dot(inverse, matrix)
        return gap, jnp.sum(gap * gap)

    def going(state):
        _, _, norm2, prev2, _, _, best2, step = state
        stalled = (norm2 < 1e-2) & (norm2 > 0.25 * prev2)
        return (step < NS_MAX_STEPS) & (best2 > NS_TOL2) & jnp.isfinite(norm2) & ~stalled

    def refine(state):
        inverse, gap, norm2, _, best, best_gap, best2, step = state
        new_inverse = inverse + dense_dot(gap, inverse)
        new_gap, new2 = residual(new_inverse)
        better = new2 < best2
        best = jnp.where(better, new_inverse, best)
        best_gap = jnp.where(better, new_gap, best_gap)
        best2 = jnp.where(better, new2, best2)
        return (new_inverse, new_gap, new2, norm2, best, best_gap, best2, step + 1)

    gap, norm2 = residual(inverse)
    state = (inverse, gap, norm2, jnp.float32(jnp.inf), inverse, gap, norm2, 0)
    _, _, _, _, best, best_gap, _, _ = lax.while_loop(going, refine, state)
    return best + dense_dot(best_gap, best)


def solve_spd(matrix, right_side):
    return dense_dot(spd_inverse(matrix), right_side)


def dense_dot(left_mat, right_mat):
    return jnp.dot(left_mat, right_mat, precision=lax.Precision.HIGHEST)


def body(window, link_ids, knot_ids, lag_steps, topology, smooth):
    n_dp = lax.axis_size("dp")
    n_tm = lax.axis_size("tm")
    device = lax.axis_index("dp") * n_tm + lax.axis_index("tm")
    devices = n_dp * n_tm
    columns = NLAG * GROUPS
    tm_rows, dp_rows, feats = window.shape
    samples = tm_rows * dp_rows
    per_knot = samples // KPD
    design, target = regressors(
        window.reshape(samples, feats), link_ids.reshape(samples), lag_steps, topology
    )
    dest = dp_rows // n_dp
    by_owner = design.reshape(tm_rows, n_dp, dest, columns).transpose(1, 0, 2, 3)
    parity = (knot_ids.reshape(samples) % KPD).astype(jnp.float32)
    side = jnp.stack([target, parity], 0).reshape(2, tm_rows, n_dp, dest).transpose(2, 0, 1, 3)
    per_owner = tm_rows * dest
    side = side.reshape(n_dp, 2, per_owner).astype(jnp.bfloat16)
    if per_owner == columns:
        parcel = jnp.concatenate([by_owner.reshape(n_dp, per_owner, columns), side], 1)
        got_all = lax.all_to_all(parcel, "dp", 0, 0, tiled=True)
        got = got_all[:, :per_owner, :].reshape(samples, columns)
        got_side = got_all[:, per_owner:, :].astype(jnp.float32)
    else:
        got = lax.all_to_all(
            by_owner.reshape(n_dp, per_owner, columns), "dp", 0, 0, tiled=True
        ).reshape(samples, columns)
        got_side = lax.all_to_all(side, "dp", 0, 0, tiled=True).astype(jnp.float32)
    got_target = got_side[:, 0, :].reshape(samples)
    got_parity = got_side[:, 1, :].reshape(samples)
    grams = []
    moments = []
    for which in range(KPD):
        weight = (got_parity == which).astype(jnp.bfloat16)
        weighted = got * weight[:, None]
        grams.append(
            jnp.einsum("sa,sb->ab", weighted, got, preferred_element_type=jnp.float32) / per_knot
        )
        scaled_target = (got_target * weight.astype(jnp.float32)).astype(jnp.bfloat16)
        moments.append(jnp.dot(scaled_target, got, preferred_element_type=jnp.float32) / per_knot)
    identity = jnp.eye(columns, dtype=jnp.float32)
    penalty_diag = jnp.diag(smooth)
    has_left = (device > 0).astype(jnp.float32)
    has_right = (device < devices - 1).astype(jnp.float32)

    def from_right(solved, stride):
        return from_behind(solved, ("dp", "tm"), -stride)

    half = columns // 2

    def transposed_dot(left_mat, right_mat):
        return lax.dot_general(
            left_mat, right_mat, (((0,), (0,)), ((), ())), precision=lax.Precision.HIGHEST
        )

    def pack(symmetric):
        return jnp.concatenate([symmetric[:half, :], symmetric[half:, half:]], 1)

    def unpack(packed):
        top = packed[:, :columns]
        lower = jnp.concatenate([top[:, half:].T, packed[:, columns:]], 1)
        return jnp.concatenate([top, lower], 0)

    def split_solve(system, left_coupling, right_coupling, forcing):
        inverse = spd_inverse(system)
        y_left = dense_dot(inverse, left_coupling)
        y_right = dense_dot(inverse, right_coupling)
        y_force = dense_dot(inverse, forcing[:, None])
        right_first = transposed_dot(right_coupling, y_right)
        left_first = transposed_dot(left_coupling, y_left)
        right_rest = transposed_dot(right_coupling, jnp.concatenate([y_left, y_force], 1))
        left_rest = transposed_dot(left_coupling, jnp.concatenate([y_right, y_force], 1))
        return (y_left, y_right, y_force), (right_first, right_rest), (left_first, left_rest)

    def update(system, forcing, from_left, from_right_side):
        first_left, rest_left = from_left
        first_right, rest_right = from_right_side
        new_system = system - first_left - first_right
        new_left = -rest_left[:, :columns]
        new_right = -rest_right[:, :columns]
        new_forcing = forcing - rest_left[:, columns] - rest_right[:, columns]
        return (new_system, new_left, new_right, new_forcing)

    def receive_right(parts, stride):
        first, rest = parts
        return unpack(from_right(pack(first), stride)), from_right(rest, stride)

    def receive_left(parts, stride):
        first, rest = parts
        return unpack(from_behind(pack(first), ("dp", "tm"), stride)), from_behind(
            rest, ("dp", "tm"), stride
        )

    even_system = grams[0] + RIDGE_TERM * identity + jnp.diag(smooth * (1.0 + has_left))
    (even_left, even_right, even_force), own_even, to_left = split_solve(
        even_system, -penalty_diag * has_left, -penalty_diag, moments[0]
    )
    odd_system = grams[1] + RIDGE_TERM * identity + jnp.diag(smooth * (1.0 + has_right))
    system, left_coupling, right_coupling, forcing = update(
        odd_system, moments[1], own_even, receive_right(to_left, 1)
    )
    height = devices.bit_length() - 1
    for section in range(height):
        stride = 1 << section
        _, to_right, to_left = split_solve(system, left_coupling, right_coupling, forcing)
        system, left_coupling, right_coupling, forcing = update(
            system, forcing, receive_left(to_right, stride), receive_right(to_left, stride)
        )
    solution = solve_spd(system, forcing[:, None])[:, 0]
    prior_odd = from_behind(solution, ("dp", "tm"), 1)
    even_knot = (
        even_force[:, 0]
        - dense_dot(even_left, prior_odd)
        - dense_dot(even_right, solution)
    )
    return jnp.stack([even_knot, solution]) * jnp.sqrt(jnp.float32(per_knot))


def solution(mesh):
    return jax.shard_map(
        body,
        mesh=mesh,
        in_specs=(P("tm", "dp", None), P("tm", "dp"), P("tm", "dp"), P(), P(), P()),
        out_specs=P(("dp", "tm"), None),
        check_vma=False,
    )
```

```python
import jax
import jax.numpy as jnp
from jax import lax
from jax.sharding import PartitionSpec as P

GROUPS = 64
NLAG = 4
WIN = 8
KPD = 2


RIDGE_TERM = 0.1


def from_behind(block, axis, distance):
    devices = range(lax.axis_size(axis))
    route = [(i - distance, i) for i in devices if i - distance in devices]
    return lax.ppermute(block, axis, route)


def regressors(frames_flat, link_rows, lag_steps, topology):
    samples, feats = frames_flat.shape
    columns = NLAG * GROUPS
    source = lax.broadcasted_iota(jnp.int32, (feats, columns), 0)
    target_col = lax.broadcasted_iota(jnp.int32, (feats, columns), 1)
    lag_of_col = jnp.repeat(lag_steps, GROUPS, total_repeat_length=columns)
    wanted = (WIN - 1 - lag_of_col)[None, :] * GROUPS + target_col % GROUPS
    picker = (source == wanted).astype(jnp.bfloat16)
    lagged = jnp.dot(frames_flat, picker, preferred_element_type=jnp.float32)
    chosen = (link_rows[:, None] == lax.broadcasted_iota(jnp.int32, (samples, GROUPS), 1)).astype(
        jnp.bfloat16
    )
    neighbour = jnp.dot(chosen, topology.astype(jnp.bfloat16), preferred_element_type=jnp.float32)
    design = (lagged * jnp.tile(neighbour, (1, NLAG))).astype(jnp.bfloat16)
    latest = frames_flat[:, (WIN - 1) * GROUPS :].astype(jnp.float32)
    target = jnp.sum(latest * chosen.astype(jnp.float32), axis=1)
    return (design, target)


NS_TOL2 = 1e-6
NS_FIXED_STEPS = 2
NS_MAX_STEPS = 40


def spd_inverse(matrix):
    size = matrix.shape[0]
    identity = jnp.eye(size, dtype=jnp.float32)
    inv_diag = 1.0 / jnp.sum(matrix * identity, axis=1)
    rows = jnp.sum(jnp.abs(matrix * inv_diag[:, None]), axis=1)
    upper = jnp.max(rows)
    lower = jnp.maximum(jnp.min(2.0 - rows), 0.0)
    inverse = identity * (inv_diag * (2.0 / (upper + lower)))[:, None]
    for _ in range(NS_FIXED_STEPS):
        inverse = inverse + dense_dot(identity - dense_dot(inverse, matrix), inverse)

    def residual(inverse):
        gap = identity - dense_dot(inverse, matrix)
        return gap, jnp.sum(gap * gap)

    def going(state):
        _, _, norm2, prev2, _, _, best2, step = state
        stalled = (norm2 < 1e-2) & (norm2 > 0.25 * prev2)
        return (step < NS_MAX_STEPS) & (best2 > NS_TOL2) & jnp.isfinite(norm2) & ~stalled

    def refine(state):
        inverse, gap, norm2, _, best, best_gap, best2, step = state
        new_inverse = inverse + dense_dot(gap, inverse)
        new_gap, new2 = residual(new_inverse)
        better = new2 < best2
        best = jnp.where(better, new_inverse, best)
        best_gap = jnp.where(better, new_gap, best_gap)
        best2 = jnp.where(better, new2, best2)
        return (new_inverse, new_gap, new2, norm2, best, best_gap, best2, step + 1)

    gap, norm2 = residual(inverse)
    state = (inverse, gap, norm2, jnp.float32(jnp.inf), inverse, gap, norm2, 0)
    _, _, _, _, best, best_gap, _, _ = lax.while_loop(going, refine, state)
    return best + dense_dot(best_gap, best)


def solve_spd(matrix, right_side):
    return dense_dot(spd_inverse(matrix), right_side)


def dense_dot(left_mat, right_mat):
    return jnp.dot(left_mat, right_mat, precision=lax.Precision.HIGHEST)


def body(window, link_ids, knot_ids, lag_steps, topology, smooth):
    n_dp = lax.axis_size("dp")
    n_tm = lax.axis_size("tm")
    device = lax.axis_index("dp") * n_tm + lax.axis_index("tm")
    devices = n_dp * n_tm
    columns = NLAG * GROUPS
    tm_rows, dp_rows, feats = window.shape
    samples = tm_rows * dp_rows
    per_knot = samples // KPD
    design, target = regressors(
        window.reshape(samples, feats), link_ids.reshape(samples), lag_steps, topology
    )
    dest = dp_rows // n_dp
    by_owner = design.reshape(tm_rows, n_dp, dest, columns).transpose(1, 0, 2, 3)
    parity = (knot_ids.reshape(samples) % KPD).astype(jnp.float32)
    side = jnp.stack([target, parity], 0).reshape(2, tm_rows, n_dp, dest).transpose(2, 0, 1, 3)
    per_owner = tm_rows * dest
    side = side.reshape(n_dp, 2, per_owner).astype(jnp.bfloat16)
    if per_owner == columns:
        parcel = jnp.concatenate([by_owner.reshape(n_dp, per_owner, columns), side], 1)
        got_all = lax.all_to_all(parcel, "dp", 0, 0, tiled=True)
        got = got_all[:, :per_owner, :].reshape(samples, columns)
        got_side = got_all[:, per_owner:, :].astype(jnp.float32)
    else:
        got = lax.all_to_all(
            by_owner.reshape(n_dp, per_owner, columns), "dp", 0, 0, tiled=True
        ).reshape(samples, columns)
        got_side = lax.all_to_all(side, "dp", 0, 0, tiled=True).astype(jnp.float32)
    got_target = got_side[:, 0, :].reshape(samples)
    got_parity = got_side[:, 1, :].reshape(samples)
    grams = []
    moments = []
    for which in range(KPD):
        weight = (got_parity == which).astype(jnp.bfloat16)
        weighted = got * weight[:, None]
        grams.append(
            jnp.einsum("sa,sb->ab", weighted, got, preferred_element_type=jnp.float32) / per_knot
        )
        scaled_target = (got_target * weight.astype(jnp.float32)).astype(jnp.bfloat16)
        moments.append(jnp.dot(scaled_target, got, preferred_element_type=jnp.float32) / per_knot)
    identity = jnp.eye(columns, dtype=jnp.float32)
    penalty_diag = jnp.diag(smooth)
    has_left = (device > 0).astype(jnp.float32)
    has_right = (device < devices - 1).astype(jnp.float32)

    def from_right(solved, stride):
        return from_behind(solved, ("dp", "tm"), -stride)

    half = columns // 2

    def transposed_dot(left_mat, right_mat):
        return lax.dot_general(
            left_mat, right_mat, (((0,), (0,)), ((), ())), precision=lax.Precision.HIGHEST
        )

    def pack(symmetric):
        return jnp.concatenate([symmetric[:half, :], symmetric[half:, half:]], 1)

    def unpack(packed):
        top = packed[:, :columns]
        lower = jnp.concatenate([top[:, half:].T, packed[:, columns:]], 1)
        return jnp.concatenate([top, lower], 0)

    def split_solve(system, left_coupling, right_coupling, forcing):
        inverse = spd_inverse(system)
        y_left = dense_dot(inverse, left_coupling)
        y_right = dense_dot(inverse, right_coupling)
        y_force = dense_dot(inverse, forcing[:, None])
        right_first = transposed_dot(right_coupling, y_right)
        left_first = transposed_dot(left_coupling, y_left)
        right_rest = transposed_dot(right_coupling, jnp.concatenate([y_left, y_force], 1))
        left_rest = transposed_dot(left_coupling, jnp.concatenate([y_right, y_force], 1))
        return (y_left, y_right, y_force), (right_first, right_rest), (left_first, left_rest)

    def update(system, forcing, from_left, from_right_side):
        first_left, rest_left = from_left
        first_right, rest_right = from_right_side
        new_system = system - first_left - first_right
        new_left = -rest_left[:, :columns]
        new_right = -rest_right[:, :columns]
        new_forcing = forcing - rest_left[:, columns] - rest_right[:, columns]
        return (new_system, new_left, new_right, new_forcing)

    def receive_right(parts, stride):
        first, rest = parts
        return unpack(from_right(pack(first), stride)), from_right(rest, stride)

    def receive_left(parts, stride):
        first, rest = parts
        return unpack(from_behind(pack(first), ("dp", "tm"), stride)), from_behind(
            rest, ("dp", "tm"), stride
        )

    even_system = grams[0] + RIDGE_TERM * identity + jnp.diag(smooth * (1.0 + has_left))
    (even_left, even_right, even_force), own_even, to_left = split_solve(
        even_system, -penalty_diag * has_left, -penalty_diag, moments[0]
    )
    odd_system = grams[1] + RIDGE_TERM * identity + jnp.diag(smooth * (1.0 + has_right))
    system, left_coupling, right_coupling, forcing = update(
        odd_system, moments[1], own_even, receive_right(to_left, 1)
    )
    height = devices.bit_length() - 1
    for section in range(height):
        stride = 1 << section
        _, to_right, to_left = split_solve(system, left_coupling, right_coupling, forcing)
        system, left_coupling, right_coupling, forcing = update(
            system, forcing, receive_left(to_right, stride), receive_right(to_left, stride)
        )
    solution = solve_spd(system, forcing[:, None])[:, 0]
    prior_odd = from_behind(solution, ("dp", "tm"), 1)
    even_knot = (
        even_force[:, 0]
        - dense_dot(even_left, prior_odd)
        - dense_dot(even_right, solution)
    )
    return jnp.stack([even_knot, solution]) * jnp.sqrt(jnp.float32(per_knot))


def solution(mesh):
    return jax.shard_map(
        body,
        mesh=mesh,
        in_specs=(P("tm", "dp", None), P("tm", "dp"), P("tm", "dp"), P(), P(), P()),
        out_specs=P(("dp", "tm"), None),
        check_vma=False,
    )
```

```python
import jax
import jax.numpy as jnp
from jax import lax
from jax.sharding import PartitionSpec as P


GROUPS = 64
NLAG = 4
WIN = 8
KPD = 2


RIDGE_TERM = 0.1


def from_behind(block, axis, distance):
    devices = range(lax.axis_size(axis))
    route = [(i - distance, i) for i in devices if i - distance in devices]
    return lax.ppermute(block, axis, route)


def regressors(frames_flat, link_rows, lag_steps, topology):
    samples, feats = frames_flat.shape
    columns = NLAG * GROUPS
    source = lax.broadcasted_iota(jnp.int32, (feats, columns), 0)
    target_col = lax.broadcasted_iota(jnp.int32, (feats, columns), 1)
    lag_of_col = jnp.repeat(lag_steps, GROUPS, total_repeat_length=columns)
    wanted = (WIN - 1 - lag_of_col)[None, :] * GROUPS + target_col % GROUPS
    picker = (source == wanted).astype(jnp.bfloat16)
    lagged = jnp.dot(frames_flat, picker, preferred_element_type=jnp.float32)
    chosen = (link_rows[:, None] == lax.broadcasted_iota(jnp.int32, (samples, GROUPS), 1)).astype(
        jnp.bfloat16
    )
    neighbour = jnp.dot(chosen, topology.astype(jnp.bfloat16), preferred_element_type=jnp.float32)
    design = (lagged * jnp.tile(neighbour, (1, NLAG))).astype(jnp.bfloat16)
    latest = frames_flat[:, (WIN - 1) * GROUPS :].astype(jnp.float32)
    target = jnp.sum(latest * chosen.astype(jnp.float32), axis=1)
    return (design, target)


NS_TOL2 = 1e-6
NS_FIXED_STEPS = 2
NS_MAX_STEPS = 40


def spd_inverse(matrix):
    size = matrix.shape[0]
    identity = jnp.eye(size, dtype=jnp.float32)
    inv_diag = 1.0 / jnp.sum(matrix * identity, axis=1)
    rows = jnp.sum(jnp.abs(matrix * inv_diag[:, None]), axis=1)
    upper = jnp.max(rows)
    lower = jnp.maximum(jnp.min(2.0 - rows), 0.0)
    inverse = identity * (inv_diag * (2.0 / (upper + lower)))[:, None]
    for _ in range(NS_FIXED_STEPS):
        inverse = inverse + dense_dot(identity - dense_dot(inverse, matrix), inverse)

    def residual(inverse):
        gap = identity - dense_dot(inverse, matrix)
        return gap, jnp.sum(gap * gap)

    def going(state):
        _, _, norm2, prev2, _, _, best2, step = state
        stalled = (norm2 < 1e-2) & (norm2 > 0.25 * prev2)
        return (step < NS_MAX_STEPS) & (best2 > NS_TOL2) & jnp.isfinite(norm2) & ~stalled

    def refine(state):
        inverse, gap, norm2, _, best, best_gap, best2, step = state
        new_inverse = inverse + dense_dot(gap, inverse)
        new_gap, new2 = residual(new_inverse)
        better = new2 < best2
        best = jnp.where(better, new_inverse, best)
        best_gap = jnp.where(better, new_gap, best_gap)
        best2 = jnp.where(better, new2, best2)
        return (new_inverse, new_gap, new2, norm2, best, best_gap, best2, step + 1)

    gap, norm2 = residual(inverse)
    state = (inverse, gap, norm2, jnp.float32(jnp.inf), inverse, gap, norm2, 0)
    _, _, _, _, best, best_gap, _, _ = lax.while_loop(going, refine, state)
    return best + dense_dot(best_gap, best)


def solve_spd(matrix, right_side):
    return dense_dot(spd_inverse(matrix), right_side)


def dense_dot(left_mat, right_mat):
    return jnp.dot(left_mat, right_mat, precision=lax.Precision.HIGHEST)


def body(window, link_ids, knot_ids, lag_steps, topology, smooth):
    n_dp = lax.axis_size("dp")
    n_tm = lax.axis_size("tm")
    device = lax.axis_index("dp") * n_tm + lax.axis_index("tm")
    devices = n_dp * n_tm
    columns = NLAG * GROUPS
    tm_rows, dp_rows, feats = window.shape
    samples = tm_rows * dp_rows
    per_knot = samples // KPD
    design, target = regressors(
        window.reshape(samples, feats), link_ids.reshape(samples), lag_steps, topology
    )
    dest = dp_rows // n_dp
    by_owner = design.reshape(tm_rows, n_dp, dest, columns).transpose(1, 0, 2, 3)
    parity = (knot_ids.reshape(samples) % KPD).astype(jnp.float32)
    side = jnp.stack([target, parity], 0).reshape(2, tm_rows, n_dp, dest).transpose(2, 0, 1, 3)
    per_owner = tm_rows * dest
    side = side.reshape(n_dp, 2, per_owner).astype(jnp.bfloat16)
    if per_owner == columns:
        parcel = jnp.concatenate([by_owner.reshape(n_dp, per_owner, columns), side], 1)
        got_all = lax.all_to_all(parcel, "dp", 0, 0, tiled=True)
        got = got_all[:, :per_owner, :].reshape(samples, columns)
        got_side = got_all[:, per_owner:, :].astype(jnp.float32)
    else:
        got = lax.all_to_all(
            by_owner.reshape(n_dp, per_owner, columns), "dp", 0, 0, tiled=True
        ).reshape(samples, columns)
        got_side = lax.all_to_all(side, "dp", 0, 0, tiled=True).astype(jnp.float32)
    got_target = got_side[:, 0, :].reshape(samples)
    got_parity = got_side[:, 1, :].reshape(samples)
    grams = []
    moments = []
    for which in range(KPD):
        weight = (got_parity == which).astype(jnp.bfloat16)
        weighted = got * weight[:, None]
        grams.append(
            jnp.einsum("sa,sb->ab", weighted, got, preferred_element_type=jnp.float32) / per_knot
        )
        scaled_target = (got_target * weight.astype(jnp.float32)).astype(jnp.bfloat16)
        moments.append(jnp.dot(scaled_target, got, preferred_element_type=jnp.float32) / per_knot)
    identity = jnp.eye(columns, dtype=jnp.float32)
    penalty_diag = jnp.diag(smooth)
    has_left = (device > 0).astype(jnp.float32)
    has_right = (device < devices - 1).astype(jnp.float32)

    def from_right(solved, stride):
        return from_behind(solved, ("dp", "tm"), -stride)

    half = columns // 2

    def transposed_dot(left_mat, right_mat):
        return lax.dot_general(
            left_mat, right_mat, (((0,), (0,)), ((), ())), precision=lax.Precision.HIGHEST
        )

    def pack(symmetric):
        return jnp.concatenate([symmetric[:half, :], symmetric[half:, half:]], 1)

    def unpack(packed):
        top = packed[:, :columns]
        lower = jnp.concatenate([top[:, half:].T, packed[:, columns:]], 1)
        return jnp.concatenate([top, lower], 0)

    def split_solve(system, left_coupling, right_coupling, forcing):
        inverse = spd_inverse(system)
        y_left = dense_dot(inverse, left_coupling)
        y_right = dense_dot(inverse, right_coupling)
        y_force = dense_dot(inverse, forcing[:, None])
        right_first = transposed_dot(right_coupling, y_right)
        left_first = transposed_dot(left_coupling, y_left)
        right_rest = transposed_dot(right_coupling, jnp.concatenate([y_left, y_force], 1))
        left_rest = transposed_dot(left_coupling, jnp.concatenate([y_right, y_force], 1))
        return (y_left, y_right, y_force), (right_first, right_rest), (left_first, left_rest)

    def update(system, forcing, from_left, from_right_side):
        first_left, rest_left = from_left
        first_right, rest_right = from_right_side
        new_system = system - first_left - first_right
        new_left = -rest_left[:, :columns]
        new_right = -rest_right[:, :columns]
        new_forcing = forcing - rest_left[:, columns] - rest_right[:, columns]
        return (new_system, new_left, new_right, new_forcing)

    def receive_right(parts, stride):
        first, rest = parts
        urgent = from_right(pack(first), stride)
        return unpack(urgent), from_right(rest, stride)

    def receive_left(parts, stride):
        first, rest = parts
        urgent = from_behind(pack(first), ("dp", "tm"), stride)
        return unpack(urgent), from_behind(rest, ("dp", "tm"), stride)

    even_system = grams[0] + RIDGE_TERM * identity + jnp.diag(smooth * (1.0 + has_left))
    (even_left, even_right, even_force), own_even, to_left = split_solve(
        even_system, -penalty_diag * has_left, -penalty_diag, moments[0]
    )
    odd_system = grams[1] + RIDGE_TERM * identity + jnp.diag(smooth * (1.0 + has_right))
    system, left_coupling, right_coupling, forcing = update(
        odd_system, moments[1], own_even, receive_right(to_left, 1)
    )
    height = devices.bit_length() - 1
    for section in range(height):
        stride = 1 << section
        _, to_right, to_left = split_solve(system, left_coupling, right_coupling, forcing)
        system, left_coupling, right_coupling, forcing = update(
            system, forcing, receive_left(to_right, stride), receive_right(to_left, stride)
        )
    solution = solve_spd(system, forcing[:, None])[:, 0]
    prior_odd = from_behind(solution, ("dp", "tm"), 1)
    even_knot = (
        even_force[:, 0]
        - dense_dot(even_left, prior_odd)
        - dense_dot(even_right, solution)
    )
    return jnp.stack([even_knot, solution]) * jnp.sqrt(jnp.float32(per_knot))


def solution(mesh):
    return jax.shard_map(
        body,
        mesh=mesh,
        in_specs=(P("tm", "dp", None), P("tm", "dp"), P("tm", "dp"), P(), P(), P()),
        out_specs=P(("dp", "tm"), None),
        check_vma=False,
    )
```

```python
import jax
import jax.numpy as jnp
from jax import lax
from jax.sharding import PartitionSpec as P

GROUPS = 64
NLAG = 4
WIN = 8
KPD = 2


RIDGE_TERM = 0.1


def from_behind(block, axis, distance):
    devices = range(lax.axis_size(axis))
    route = [(i - distance, i) for i in devices if i - distance in devices]
    return lax.ppermute(block, axis, route)


def regressors(frames_flat, link_rows, lag_steps, topology):
    samples, feats = frames_flat.shape
    columns = NLAG * GROUPS
    source = lax.broadcasted_iota(jnp.int32, (feats, columns), 0)
    target_col = lax.broadcasted_iota(jnp.int32, (feats, columns), 1)
    lag_of_col = jnp.repeat(lag_steps, GROUPS, total_repeat_length=columns)
    wanted = (WIN - 1 - lag_of_col)[None, :] * GROUPS + target_col % GROUPS
    picker = (source == wanted).astype(jnp.bfloat16)
    lagged = jnp.dot(frames_flat, picker, preferred_element_type=jnp.float32)
    chosen = (link_rows[:, None] == lax.broadcasted_iota(jnp.int32, (samples, GROUPS), 1)).astype(
        jnp.bfloat16
    )
    neighbour = jnp.dot(chosen, topology.astype(jnp.bfloat16), preferred_element_type=jnp.float32)
    design = (lagged * jnp.tile(neighbour, (1, NLAG))).astype(jnp.bfloat16)
    latest = frames_flat[:, (WIN - 1) * GROUPS :].astype(jnp.float32)
    target = jnp.sum(latest * chosen.astype(jnp.float32), axis=1)
    return (design, target)


NS_TOL2 = 1e-6
NS_FIXED_STEPS = 2
NS_MAX_STEPS = 40


def spd_inverse(matrix):
    size = matrix.shape[0]
    identity = jnp.eye(size, dtype=jnp.float32)
    inv_diag = 1.0 / jnp.sum(matrix * identity, axis=1)
    rows = jnp.sum(jnp.abs(matrix * inv_diag[:, None]), axis=1)
    upper = jnp.max(rows)
    lower = jnp.maximum(jnp.min(2.0 - rows), 0.0)
    inverse = identity * (inv_diag * (2.0 / (upper + lower)))[:, None]
    for _ in range(NS_FIXED_STEPS):
        inverse = inverse + dense_dot(identity - dense_dot(inverse, matrix), inverse)

    def residual(inverse):
        gap = identity - dense_dot(inverse, matrix)
        return gap, jnp.sum(gap * gap)

    def going(state):
        _, _, norm2, step, done = state
        return (step < NS_MAX_STEPS) & (norm2 > NS_TOL2) & ~done

    def refine(state):
        inverse, gap, norm2, step, _ = state
        trial = inverse + dense_dot(gap, inverse)
        trial_gap, trial2 = residual(trial)
        better = trial2 < norm2
        stalled = (trial2 < 1e-2) & (trial2 > 0.25 * norm2)
        inverse = jnp.where(better, trial, inverse)
        gap = jnp.where(better, trial_gap, gap)
        norm2 = jnp.where(better, trial2, norm2)
        return (inverse, gap, norm2, step + 1, ~better | stalled)

    gap, norm2 = residual(inverse)
    best, best_gap, _, _, _ = lax.while_loop(
        going, refine, (inverse, gap, norm2, 0, ~jnp.isfinite(norm2))
    )
    return best + dense_dot(best_gap, best)


def solve_spd(matrix, right_side):
    return dense_dot(spd_inverse(matrix), right_side)


def dense_dot(left_mat, right_mat):
    return jnp.dot(left_mat, right_mat, precision=lax.Precision.HIGHEST)


def body(window, link_ids, knot_ids, lag_steps, topology, smooth):
    n_dp = lax.axis_size("dp")
    n_tm = lax.axis_size("tm")
    device = lax.axis_index("dp") * n_tm + lax.axis_index("tm")
    devices = n_dp * n_tm
    columns = NLAG * GROUPS
    tm_rows, dp_rows, feats = window.shape
    samples = tm_rows * dp_rows
    per_knot = samples // KPD
    design, target = regressors(
        window.reshape(samples, feats), link_ids.reshape(samples), lag_steps, topology
    )
    dest = dp_rows // n_dp
    by_owner = design.reshape(tm_rows, n_dp, dest, columns).transpose(1, 0, 2, 3)
    parity = (knot_ids.reshape(samples) % KPD).astype(jnp.float32)
    side = jnp.stack([target, parity], 0).reshape(2, tm_rows, n_dp, dest).transpose(2, 0, 1, 3)
    per_owner = tm_rows * dest
    side = side.reshape(n_dp, 2, per_owner).astype(jnp.bfloat16)
    if per_owner == columns:
        parcel = jnp.concatenate([by_owner.reshape(n_dp, per_owner, columns), side], 1)
        got_all = lax.all_to_all(parcel, "dp", 0, 0, tiled=True)
        got = got_all[:, :per_owner, :].reshape(samples, columns)
        got_side = got_all[:, per_owner:, :].astype(jnp.float32)
    else:
        got = lax.all_to_all(
            by_owner.reshape(n_dp, per_owner, columns), "dp", 0, 0, tiled=True
        ).reshape(samples, columns)
        got_side = lax.all_to_all(side, "dp", 0, 0, tiled=True).astype(jnp.float32)
    got_target = got_side[:, 0, :].reshape(samples)
    got_parity = got_side[:, 1, :].reshape(samples)
    grams = []
    moments = []
    for which in range(KPD):
        weight = (got_parity == which).astype(jnp.bfloat16)
        weighted = got * weight[:, None]
        grams.append(
            jnp.einsum("sa,sb->ab", weighted, got, preferred_element_type=jnp.float32) / per_knot
        )
        scaled_target = (got_target * weight.astype(jnp.float32)).astype(jnp.bfloat16)
        moments.append(jnp.dot(scaled_target, got, preferred_element_type=jnp.float32) / per_knot)
    identity = jnp.eye(columns, dtype=jnp.float32)
    penalty_diag = jnp.diag(smooth)
    has_left = (device > 0).astype(jnp.float32)
    has_right = (device < devices - 1).astype(jnp.float32)

    def from_right(solved, stride):
        return from_behind(solved, ("dp", "tm"), -stride)

    half = columns // 2

    def transposed_dot(left_mat, right_mat):
        return lax.dot_general(
            left_mat, right_mat, (((0,), (0,)), ((), ())), precision=lax.Precision.HIGHEST
        )

    def pack(symmetric):
        return jnp.concatenate([symmetric[:half, :], symmetric[half:, half:]], 1)

    def unpack(packed):
        top = packed[:, :columns]
        lower = jnp.concatenate([top[:, half:].T, packed[:, columns:]], 1)
        return jnp.concatenate([top, lower], 0)

    def split_solve(system, left_coupling, right_coupling, forcing):
        inverse = spd_inverse(system)
        y_left = dense_dot(inverse, left_coupling)
        y_right = dense_dot(inverse, right_coupling)
        y_force = dense_dot(inverse, forcing[:, None])
        right_first = transposed_dot(right_coupling, y_right)
        left_first = transposed_dot(left_coupling, y_left)
        right_rest = transposed_dot(right_coupling, jnp.concatenate([y_left, y_force], 1))
        left_rest = transposed_dot(left_coupling, jnp.concatenate([y_right, y_force], 1))
        return (y_left, y_right, y_force), (right_first, right_rest), (left_first, left_rest)

    def update(system, forcing, from_left, from_right_side):
        first_left, rest_left = from_left
        first_right, rest_right = from_right_side
        new_system = system - first_left - first_right
        new_left = -rest_left[:, :columns]
        new_right = -rest_right[:, :columns]
        new_forcing = forcing - rest_left[:, columns] - rest_right[:, columns]
        return (new_system, new_left, new_right, new_forcing)

    def receive_right(parts, stride):
        first, rest = parts
        return unpack(from_right(pack(first), stride)), from_right(rest, stride)

    def receive_left(parts, stride):
        first, rest = parts
        return unpack(from_behind(pack(first), ("dp", "tm"), stride)), from_behind(
            rest, ("dp", "tm"), stride
        )

    even_system = grams[0] + RIDGE_TERM * identity + jnp.diag(smooth * (1.0 + has_left))
    (even_left, even_right, even_force), own_even, to_left = split_solve(
        even_system, -penalty_diag * has_left, -penalty_diag, moments[0]
    )
    odd_system = grams[1] + RIDGE_TERM * identity + jnp.diag(smooth * (1.0 + has_right))
    system, left_coupling, right_coupling, forcing = update(
        odd_system, moments[1], own_even, receive_right(to_left, 1)
    )
    height = devices.bit_length() - 1
    for section in range(height):
        stride = 1 << section
        _, to_right, to_left = split_solve(system, left_coupling, right_coupling, forcing)
        system, left_coupling, right_coupling, forcing = update(
            system, forcing, receive_left(to_right, stride), receive_right(to_left, stride)
        )
    solution = solve_spd(system, forcing[:, None])[:, 0]
    prior_odd = from_behind(solution, ("dp", "tm"), 1)
    even_knot = (
        even_force[:, 0]
        - dense_dot(even_left, prior_odd)
        - dense_dot(even_right, solution)
    )
    return jnp.stack([even_knot, solution]) * jnp.sqrt(jnp.float32(per_knot))


def solution(mesh):
    return jax.shard_map(
        body,
        mesh=mesh,
        in_specs=(P("tm", "dp", None), P("tm", "dp"), P("tm", "dp"), P(), P(), P()),
        out_specs=P(("dp", "tm"), None),
        check_vma=False,
    )
```
